32 devices in a mesh: dp: 16 (over z, x, core), group: 2 (over y).
Axes of the slice: x: 2, y: 2, z: 4, core: 2. Of those that a mesh axis runs over, the one named last changes fastest.
Arguments:
- inputs: bfloat16 [32768, 2048], P('dp', 'group'), may hold values from -6 to 6
- grad_out: bfloat16 [32768, 2048], P(('dp', 'group')), may hold values from -0.0625 to 0.0625
- weight: bfloat16 [2048, 2048], P('group'), may hold values from -6 to 6
- old_basis: float32 [2048, 256], P('group'), may hold values from -0.125 to 0.125
- first_moment: float32 [256, 2048], P(None, 'dp'), may hold values from -6 to 6
- second_moment: float32 [256, 2048], P(None, 'dp'), may hold values from 0.1 to 3
Outputs:
- new_weight: bfloat16 [2048, 2048], P('group')
- new_first: float32 [256, 2048], P(None, 'dp')
- new_second: float32 [256, 2048], P(None, 'dp')
- new_basis: float32 [2048, 256], P('group')
The draws below stay inside these ranges and needn't reach their ends.
All inputs are finite; a program needn't handle non-finite values.
Results may differ from the reference program's by a relative error of at most 0.011.
Values may be sent and summed in bfloat16 or wider, within the bound.
No kernel may reach another device: no remote copies, remote signals or barrier semaphores. Data moves between devices by JAX's collectives and lax.ppermute only.
A program may use at most 64 MiB of HBM per device.

```python
import math
import jax
import jax.numpy as jnp
from jax import lax

D = 2048
RANK = 256
NS_STEPS = 5
STEP = 10
TOKENS = 32768


def strengthened(drawn, stream_key, source, target, blocks, factor):
    owner, partner = [(jnp.arange(drawn.shape[position]) // (drawn.shape[position] // blocks)).reshape([-1 if axis == position else 1 for axis in range(drawn.ndim)]) for position in (source, target)]
    chosen = jax.random.permutation(stream_key, blocks)[partner]
    strong = (owner == chosen) | (owner == (partner + blocks // 2) % blocks)
    return jnp.where(strong, factor * drawn, drawn)


def block_scale(stream_key, extent, cuts, least, largest):
    def one(position, parts):
        draws = jax.random.uniform(jax.random.fold_in(jax.random.fold_in(stream_key, 6), position), (parts,), jnp.float32, least / len(cuts), largest / len(cuts))
        return jnp.repeat(jnp.exp(draws), extent[position] // parts).reshape((-1,) + (1,) * (len(extent) - position - 1))

    loudness = one(*cuts[0])
    for cut in cuts[1:]:
        loudness = loudness * one(*cut)
    return loudness


def centred(stream_key, extent, width, bound, pieces=(), kind=jnp.bfloat16):
    gain = block_scale(stream_key, extent, pieces, -0.22, 0.18) if pieces else 1.0
    array = jax.random.normal(stream_key, extent, jnp.float32) * width * gain
    return jnp.minimum(jnp.maximum(array, -bound), bound).astype(kind)


def bell_draw_with(key, extent, spread, most, shards, heavy, dtype=jnp.bfloat16):
    array = spread * jax.random.normal(key, extent, jnp.float32)
    if shards:
        array = array * block_scale(key, extent, shards, -0.22, 0.18)
    return jnp.clip(strengthened(array, jax.random.fold_in(key, 3), *heavy), -most, most).astype(dtype)


def setup_inputs(seed: int = 0) -> dict:
    key_of = jax.random.split(jax.random.key(seed), 7)
    return {
        "inputs": centred(key_of[0], (TOKENS, D), 1.0, 6.0, ((0, 16), (1, 2))),
        "grad_out": bell_draw_with(key_of[1], (TOKENS, D), (1.0 / TOKENS ** 0.5), 0.0625, ((0, 32),), (0, 1, 32, 2.75)),
        "weight": centred(key_of[2], (D, D), 1.0, 6.0, ((0, 2),)),
        "old_basis": centred(key_of[3], (D, RANK), D ** -0.5, 0.125, ((0, 2),), jnp.float32),
        "first_moment": centred(key_of[4], (RANK, D), 1.0, 6.0, ((1, 16),), jnp.float32),
        "second_moment": jnp.clip(jnp.exp(math.log(3.0) - 3.4011974 * jax.random.uniform(key_of[5], (RANK, D), jnp.float32) ** block_scale(key_of[5], (RANK, D), ((1, 16),), -0.2, 0.2)), 0.1, 3.0),
    }


BETA_ONE = 0.9
BETA_TWO = 0.99
ADAM_EPS = 1e-08
HIGHEST = lax.Precision.HIGHEST

def reference(inputs, grad_out, weight, old_basis, first_moment, second_moment):
    gradient = jnp.dot(inputs.T, grad_out, preferred_element_type=jnp.float32)
    projected = jnp.dot(old_basis.T, gradient, precision=HIGHEST)
    new_first = BETA_ONE * first_moment + (1.0 - BETA_ONE) * projected
    new_second = BETA_TWO * second_moment + (1.0 - BETA_TWO) * projected * projected
    direction = new_first / (1.0 - BETA_ONE ** STEP) / (jnp.sqrt(new_second / (1.0 - BETA_TWO ** STEP)) + ADAM_EPS)
    change = jnp.dot(old_basis, direction, precision=HIGHEST)
    new_weight = (weight.astype(jnp.float32) - change).astype(jnp.bfloat16)
    subspace = jnp.dot(gradient, projected.T, precision=HIGHEST)
    iterate = subspace / jnp.sqrt(jnp.sum(subspace * subspace))
    for sweep in range(NS_STEPS):
        gram = jnp.dot(iterate.T, iterate, precision=HIGHEST)
        iterate = 1.5 * iterate - 0.5 * jnp.dot(iterate, gram, precision=HIGHEST)
    return (new_weight, new_first, new_second, iterate)
```

```python
import jax
import jax.numpy as jnp
from jax import lax
from jax.sharding import PartitionSpec as P

NS_STEPS = 5
STEP = 10


BETA_ONE = 0.9
BETA_TWO = 0.99
ADAM_EPS = 1e-08
HIGHEST = lax.Precision.HIGHEST
F32 = jnp.float32
BF16 = jnp.bfloat16


def matmul(left, right):
    return jnp.dot(left, right, precision=HIGHEST)


def split(value):
    high = value.astype(BF16)
    return high, (value - high.astype(F32)).astype(BF16)


def dot_mixed(left, right, dims):
    def one(a, b):
        return lax.dot_general(a, b, (dims, ((), ())), preferred_element_type=F32)

    if left.dtype == F32:
        high, low = split(left)
        return one(high, right) + one(low, right)
    high, low = split(right)
    return one(left, high) + one(left, low)


def log2(n):
    bits = n.bit_length() - 1
    assert 1 << bits == n
    return bits


def swap(x, axis, n, bit):
    return lax.ppermute(x, axis, [(k, k ^ (1 << bit)) for k in range(n)])


def reduce_scatter(x, axis, n, dim, order):
    levels = log2(n)
    me = lax.axis_index(axis)
    shape = x.shape
    block = shape[dim] // n
    x = x.reshape(shape[:dim] + (2,) * levels + (block,) + shape[dim + 1 :])
    remaining = list(range(levels - 1, -1, -1))
    for bit in order:
        pos = dim + remaining.index(bit)
        mine = (me >> bit) & 1
        keep = lax.dynamic_index_in_dim(x, mine, axis=pos, keepdims=False)
        send = lax.dynamic_index_in_dim(x, 1 - mine, axis=pos, keepdims=False)
        x = keep + swap(send, axis, n, bit)
        remaining.remove(bit)
    return x.reshape(shape[:dim] + (block,) + shape[dim + 1 :])


def all_gather(x, axis, n, dim, order):
    me = lax.axis_index(axis)
    shape = x.shape
    present = []
    for bit in order:
        other = swap(x, axis, n, bit)
        first = ((me >> bit) & 1) == 0
        low = jnp.where(first, x, other)
        high = jnp.where(first, other, x)
        present = sorted(present + [bit], reverse=True)
        x = jnp.stack([low, high], axis=dim + present.index(bit))
    return x.reshape(shape[:dim] + (n * shape[dim],) + shape[dim + 1 :])


def all_reduce(x, axis, n):
    for bit in range(log2(n)):
        x = x + swap(x, axis, n, bit)
    return x


def make_shards(dp_count, group_count):
    dp_up = list(range(log2(dp_count)))
    dp_down = dp_up[::-1]
    group_up = list(range(log2(group_count)))
    group_down = group_up[::-1]

    def shards(inputs, grad_out, weight, old_basis, first_moment, second_moment):
        basis_high, basis_low = split(old_basis)
        tokens_basis = lax.dot_general(
            inputs, basis_high, (((1,), (0,)), ((), ())), preferred_element_type=F32
        ) + lax.dot_general(inputs, basis_low, (((1,), (0,)), ((), ())), preferred_element_type=F32)
        tokens_basis = reduce_scatter(tokens_basis, "group", group_count, 0, group_up)
        projected_part = dot_mixed(tokens_basis, grad_out, ((0,), (0,)))
        projected = reduce_scatter(projected_part, "dp", dp_count, 1, dp_up)
        projected = all_reduce(projected, "group", group_count)

        new_first = BETA_ONE * first_moment + (1.0 - BETA_ONE) * projected
        new_second = BETA_TWO * second_moment + (1.0 - BETA_TWO) * projected * projected
        direction = (
            new_first
            / (1.0 - BETA_ONE**STEP)
            / (jnp.sqrt(new_second / (1.0 - BETA_TWO**STEP)) + ADAM_EPS)
        )

        projected_all = all_gather(projected, "dp", dp_count, 1, dp_down)
        direction_all = all_gather(direction, "dp", dp_count, 1, dp_down)

        tokens_sub = dot_mixed(grad_out, projected_all, ((1,), (1,)))
        tokens_sub = all_gather(tokens_sub, "group", group_count, 0, group_down)
        subspace_part = dot_mixed(inputs, tokens_sub, ((0,), (0,)))
        subspace = reduce_scatter(subspace_part, "dp", dp_count, 0, dp_up)
        subspace = all_gather(subspace, "dp", dp_count, 0, dp_down)

        gram = lax.dot_general(subspace, subspace, (((0,), (0,)), ((), ())), precision=HIGHEST)
        gram = all_reduce(gram, "group", group_count)
        squares = jnp.trace(gram)
        current = gram / squares
        eye = jnp.eye(gram.shape[0], dtype=F32)
        product = None
        for sweep in range(NS_STEPS):
            step = 1.5 * eye - 0.5 * current
            product = step if product is None else matmul(product, step)
            if sweep + 1 < NS_STEPS:
                current = matmul(step, matmul(current, step))
        new_basis = matmul(subspace / jnp.sqrt(squares), product)

        change = matmul(old_basis, direction_all)
        new_weight = (weight.astype(F32) - change).astype(BF16)
        return (new_weight, new_first, new_second, new_basis)

    return shards


def solution(mesh):
    return jax.shard_map(
        make_shards(mesh.shape["dp"], mesh.shape["group"]),
        mesh=mesh,
        in_specs=(
            P("dp", "group"),
            P(("dp", "group"), None),
            P("group", None),
            P("group", None),
            P(None, "dp"),
            P(None, "dp"),
        ),
        out_specs=(P("group", None), P(None, "dp"), P(None, "dp"), P("group", None)),
        check_vma=False,
    )
```

```python
import jax
import jax.numpy as jnp
from jax import lax
from jax.sharding import PartitionSpec as P

NS_STEPS = 5
STEP = 10


BETA_ONE = 0.9
BETA_TWO = 0.99
ADAM_EPS = 1e-08
HIGHEST = lax.Precision.HIGHEST
F32 = jnp.float32
BF16 = jnp.bfloat16


def matmul(left, right):
    return jnp.dot(left, right, precision=HIGHEST)


def split(value):
    high = value.astype(BF16)
    return high, (value - high.astype(F32)).astype(BF16)


def dot_mixed(left, right, dims):
    def one(a, b):
        return lax.dot_general(a, b, (dims, ((), ())), preferred_element_type=F32)

    if left.dtype == F32:
        high, low = split(left)
        return one(high, right) + one(low, right)
    high, low = split(right)
    return one(left, high) + one(left, low)


def log2(n):
    bits = n.bit_length() - 1
    assert 1 << bits == n
    return bits


def swap(x, axis, n, bit):
    return lax.ppermute(x, axis, [(k, k ^ (1 << bit)) for k in range(n)])


def reduce_scatter(x, axis, n, dim, order):
    levels = log2(n)
    me = lax.axis_index(axis)
    shape = x.shape
    block = shape[dim] // n
    x = x.reshape(shape[:dim] + (2,) * levels + (block,) + shape[dim + 1 :])
    remaining = list(range(levels - 1, -1, -1))
    for bit in order:
        pos = dim + remaining.index(bit)
        mine = (me >> bit) & 1
        keep = lax.dynamic_index_in_dim(x, mine, axis=pos, keepdims=False)
        send = lax.dynamic_index_in_dim(x, 1 - mine, axis=pos, keepdims=False)
        x = keep + swap(send, axis, n, bit)
        remaining.remove(bit)
    return x.reshape(shape[:dim] + (block,) + shape[dim + 1 :])


def all_gather(x, axis, n, dim, order):
    me = lax.axis_index(axis)
    shape = x.shape
    present = []
    for bit in order:
        other = swap(x, axis, n, bit)
        first = ((me >> bit) & 1) == 0
        low = jnp.where(first, x, other)
        high = jnp.where(first, other, x)
        present = sorted(present + [bit], reverse=True)
        x = jnp.stack([low, high], axis=dim + present.index(bit))
    return x.reshape(shape[:dim] + (n * shape[dim],) + shape[dim + 1 :])


def all_reduce(x, axis, n):
    for bit in range(log2(n)):
        x = x + swap(x, axis, n, bit)
    return x


def make_shards(dp_count, group_count):
    dp_up = list(range(log2(dp_count)))
    dp_down = dp_up[::-1]
    group_up = list(range(log2(group_count)))
    group_down = group_up[::-1]

    def shards(inputs, grad_out, weight, old_basis, first_moment, second_moment):
        basis_high, basis_low = split(old_basis)
        tokens_basis = lax.dot_general(
            inputs, basis_high, (((1,), (0,)), ((), ())), preferred_element_type=F32
        ) + lax.dot_general(inputs, basis_low, (((1,), (0,)), ((), ())), preferred_element_type=F32)
        tokens_basis = reduce_scatter(
            tokens_basis.astype(BF16), "group", group_count, 0, group_up
        ).astype(F32)
        projected_part = dot_mixed(tokens_basis, grad_out, ((0,), (0,)))
        projected = reduce_scatter(projected_part, "dp", dp_count, 1, dp_up)
        projected = all_reduce(projected, "group", group_count)

        new_first = BETA_ONE * first_moment + (1.0 - BETA_ONE) * projected
        new_second = BETA_TWO * second_moment + (1.0 - BETA_TWO) * projected * projected
        direction = (
            new_first
            / (1.0 - BETA_ONE**STEP)
            / (jnp.sqrt(new_second / (1.0 - BETA_TWO**STEP)) + ADAM_EPS)
        )

        projected_all = all_gather(projected, "dp", dp_count, 1, dp_down)
        direction_all = all_gather(direction.T, "dp", dp_count, 0, dp_down)

        tokens_sub = dot_mixed(grad_out, projected_all, ((1,), (1,)))
        tokens_sub = all_gather(tokens_sub.astype(BF16), "group", group_count, 0, group_down)
        subspace_part = dot_mixed(inputs, tokens_sub, ((0,), (0,)))
        subspace = reduce_scatter(subspace_part, "dp", dp_count, 0, dp_up)
        subspace = all_gather(subspace, "dp", dp_count, 0, dp_down)

        gram = lax.dot_general(subspace, subspace, (((0,), (0,)), ((), ())), precision=HIGHEST)
        gram = all_reduce(gram, "group", group_count)
        squares = jnp.trace(gram)
        current = gram / squares
        eye = jnp.eye(gram.shape[0], dtype=F32)
        product = None
        for sweep in range(NS_STEPS):
            step = 1.5 * eye - 0.5 * current
            product = step if product is None else matmul(product, step)
            if sweep + 1 < NS_STEPS:
                current = matmul(step, matmul(current, step))
        new_basis = matmul(subspace / jnp.sqrt(squares), product)

        direction_high, direction_low = split(direction_all)
        rows = (((1,), (1,)), ((), ()))
        change = (
            lax.dot_general(basis_high, direction_high, rows, preferred_element_type=F32)
            + lax.dot_general(basis_low, direction_high, rows, preferred_element_type=F32)
            + lax.dot_general(basis_high, direction_low, rows, preferred_element_type=F32)
        )
        new_weight = (weight.astype(F32) - change).astype(BF16)
        return (new_weight, new_first, new_second, new_basis)

    return shards


def solution(mesh):
    return jax.shard_map(
        make_shards(mesh.shape["dp"], mesh.shape["group"]),
        mesh=mesh,
        in_specs=(
            P("dp", "group"),
            P(("dp", "group"), None),
            P("group", None),
            P("group", None),
            P(None, "dp"),
            P(None, "dp"),
        ),
        out_specs=(P("group", None), P(None, "dp"), P(None, "dp"), P("group", None)),
        check_vma=False,
    )
```

```python
import jax
import jax.numpy as jnp
from jax import lax
from jax.sharding import PartitionSpec as P

NS_STEPS = 5
STEP = 10


BETA_ONE = 0.9
BETA_TWO = 0.99
ADAM_EPS = 1e-08
HIGHEST = lax.Precision.HIGHEST
F32 = jnp.float32
BF16 = jnp.bfloat16


def matmul(left, right):
    return jnp.dot(left, right, precision=HIGHEST)


def split(value):
    high = value.astype(BF16)
    return high, (value - high.astype(F32)).astype(BF16)


def dot_mixed(left, right, dims):
    def one(a, b):
        return lax.dot_general(a, b, (dims, ((), ())), preferred_element_type=F32)

    if left.dtype == F32:
        high, low = split(left)
        return one(high, right) + one(low, right)
    high, low = split(right)
    return one(left, high) + one(left, low)


def log2(n):
    bits = n.bit_length() - 1
    assert 1 << bits == n
    return bits


def swap(x, axis, n, bit):
    return lax.ppermute(x, axis, [(k, k ^ (1 << bit)) for k in range(n)])


def reduce_scatter(x, axis, n, dim, order):
    levels = log2(n)
    me = lax.axis_index(axis)
    shape = x.shape
    block = shape[dim] // n
    x = x.reshape(shape[:dim] + (2,) * levels + (block,) + shape[dim + 1 :])
    remaining = list(range(levels - 1, -1, -1))
    for bit in order:
        pos = dim + remaining.index(bit)
        mine = (me >> bit) & 1
        keep = lax.dynamic_index_in_dim(x, mine, axis=pos, keepdims=False)
        send = lax.dynamic_index_in_dim(x, 1 - mine, axis=pos, keepdims=False)
        x = keep + swap(send, axis, n, bit)
        remaining.remove(bit)
    return x.reshape(shape[:dim] + (block,) + shape[dim + 1 :])


def all_gather(x, axis, n, dim, order):
    me = lax.axis_index(axis)
    shape = x.shape
    present = []
    for bit in order:
        other = swap(x, axis, n, bit)
        first = ((me >> bit) & 1) == 0
        low = jnp.where(first, x, other)
        high = jnp.where(first, other, x)
        present = sorted(present + [bit], reverse=True)
        x = jnp.stack([low, high], axis=dim + present.index(bit))
    return x.reshape(shape[:dim] + (n * shape[dim],) + shape[dim + 1 :])


def all_reduce(x, axis, n):
    for bit in range(log2(n)):
        x = x + swap(x, axis, n, bit)
    return x


def make_shards(dp_count, group_count):
    dp_up = list(range(log2(dp_count)))
    dp_down = dp_up[::-1]
    group_up = list(range(log2(group_count)))
    group_down = group_up[::-1]

    def shards(inputs, grad_out, weight, old_basis, first_moment, second_moment):
        basis_high, basis_low = split(old_basis)
        tokens_basis = lax.dot_general(
            inputs, basis_high, (((1,), (0,)), ((), ())), preferred_element_type=F32
        ) + lax.dot_general(inputs, basis_low, (((1,), (0,)), ((), ())), preferred_element_type=F32)
        tokens_basis = reduce_scatter(
            tokens_basis.astype(BF16), "group", group_count, 0, group_up
        ).astype(F32)
        projected_part = dot_mixed(grad_out, tokens_basis, ((0,), (0,)))
        projected_rows = reduce_scatter(projected_part, "dp", dp_count, 0, dp_up)
        projected_rows = all_reduce(projected_rows, "group", group_count)
        projected = projected_rows.T

        new_first = BETA_ONE * first_moment + (1.0 - BETA_ONE) * projected
        new_second = BETA_TWO * second_moment + (1.0 - BETA_TWO) * projected * projected
        direction = (
            new_first
            / (1.0 - BETA_ONE**STEP)
            / (jnp.sqrt(new_second / (1.0 - BETA_TWO**STEP)) + ADAM_EPS)
        )

        projected_all = all_gather(projected_rows, "dp", dp_count, 0, dp_down)
        direction_all = all_gather(direction.T, "dp", dp_count, 0, dp_down)

        tokens_sub = dot_mixed(grad_out, projected_all, ((1,), (0,)))
        tokens_sub = all_gather(tokens_sub.astype(BF16), "group", group_count, 0, group_down)
        subspace_part = dot_mixed(inputs, tokens_sub, ((0,), (0,)))
        subspace = reduce_scatter(subspace_part, "dp", dp_count, 0, dp_up)
        subspace = all_gather(subspace, "dp", dp_count, 0, dp_down)

        gram = lax.dot_general(subspace, subspace, (((0,), (0,)), ((), ())), precision=HIGHEST)
        gram = all_reduce(gram, "group", group_count)
        squares = jnp.trace(gram)
        current = gram / squares
        eye = jnp.eye(gram.shape[0], dtype=F32)
        product = None
        for sweep in range(NS_STEPS):
            step = 1.5 * eye - 0.5 * current
            product = step if product is None else matmul(product, step)
            if sweep + 1 < NS_STEPS:
                current = matmul(step, matmul(current, step))
        new_basis = matmul(subspace / jnp.sqrt(squares), product)

        direction_high, direction_low = split(direction_all)
        rows = (((1,), (1,)), ((), ()))
        change = (
            lax.dot_general(basis_high, direction_high, rows, preferred_element_type=F32)
            + lax.dot_general(basis_low, direction_high, rows, preferred_element_type=F32)
            + lax.dot_general(basis_high, direction_low, rows, preferred_element_type=F32)
        )
        new_weight = (weight.astype(F32) - change).astype(BF16)
        return (new_weight, new_first, new_second, new_basis)

    return shards


def solution(mesh):
    return jax.shard_map(
        make_shards(mesh.shape["dp"], mesh.shape["group"]),
        mesh=mesh,
        in_specs=(
            P("dp", "group"),
            P(("dp", "group"), None),
            P("group", None),
            P("group", None),
            P(None, "dp"),
            P(None, "dp"),
        ),
        out_specs=(P("group", None), P(None, "dp"), P(None, "dp"), P("group", None)),
        check_vma=False,
    )
```
